32 devices in a mesh: groups: 2 (over x), chan: 16 (over z, y, core).
Axes of the slice: x: 2, y: 2, z: 4, core: 2. Of those that a mesh axis runs over, the one named last changes fastest.
Arguments:
- traces: float32 [2048, 1152], P(('groups', 'chan')), parts along dimension 0, as said below
- good_mask: int32 [2048], P(('groups', 'chan')), parts along dimension 0, may hold values 0 or 1
Outputs:
- correlations: bfloat16 [2048, 64, 1024], P(('groups', 'chan')), parts along dimension 0
The draws below stay inside these ranges and needn't reach their ends.
There are 2 independent parts, one for each index of `groups`. The reference program is written for one: setup_inputs(seed, part) draws one part's arguments, and reference() takes and returns one part's arrays. A program takes and returns all parts, laid end to end along the dimension named above; each array names one. Nothing has to cross between parts.
Inputs may be any that keep to these rules, and one draw needn't show every extreme that they name: `traces`: traces of order one.
All inputs are finite; a program needn't handle non-finite values. No bound on the sum of `good_mask` on one device may be relied on, other than what follows from the above.
Results may differ from the reference program's by a relative error of at most 0.0053.
Values may be sent and summed in bfloat16 or wider, within the bound.
No kernel may reach another device: no remote copies, remote signals or barrier semaphores. Data moves between devices by JAX's collectives and lax.ppermute only.
A program may use at most 128 MiB of HBM per device.

```python
import math
import jax
import jax.numpy as jnp
from jax import lax

CH_DEV = 64
CHANNELS = 1024
NW = 256
NF = 128
HOP = 128
LAGS = 64
NWIN = 8
SAMPLES = 1152


def draw_traces(key, part):
    key_common = jax.random.fold_in(key, 11)
    key_noise = jax.random.fold_in(key, 12)
    position = jnp.arange(CHANNELS).astype(jnp.float32) / CHANNELS
    gain = 1.0 + 2.0 * position
    common = jax.random.normal(key_common, (SAMPLES,), jnp.float32)
    noise = jax.random.normal(key_noise, (CHANNELS, SAMPLES), jnp.float32)
    return gain[:, None] * (1.5 * common[None, :] + noise)


def touch_ends(entries, key, least, largest):
    longest = entries.shape.index(max(entries.shape))
    spots = []
    for shift in (0, 1):
        where = [jax.random.randint(jax.random.fold_in(key, axis), (), 0, length) for axis, length in enumerate(entries.shape)]
        where[longest] = (where[longest] + shift) % entries.shape[longest]
        spots.append(tuple(where))
    return entries.at[spots[0]].set(least).at[spots[1]].set(largest)


def setup_inputs(seed: int = 0, part: int = 0) -> dict:
    key_of = jax.random.split(jax.random.key(seed), 3)
    part_keys = jax.random.split(jax.random.fold_in(key_of[2], part), 3)
    return {
        "traces": draw_traces(jax.random.fold_in(jax.random.fold_in(key_of[2], part), 71), part),
        "good_mask": touch_ends((jax.random.randint(part_keys[1], (CHANNELS,), 0, 8) < 7).astype(jnp.int32), jax.random.fold_in(part_keys[1], 1), 0, 1),
    }


def whiten_all(traces, good_mask):
    good = good_mask.astype(jnp.float32)
    count = jnp.sum(good)
    common = lax.optimization_barrier(jnp.sum(traces * good[:, None], axis=0)) / jnp.maximum(count, 1.0)
    clean = (traces - common[None, :]) * good[:, None]
    halves = clean.reshape(CHANNELS, NWIN + 1, HOP)
    segments = jnp.concatenate([halves[:, :-1], halves[:, 1:]], axis=2)
    samples = jnp.arange(NW).astype(jnp.float32)
    hann = 0.5 - 0.5 * jnp.cos(2.0 * math.pi * samples / NW)
    spectrum = jnp.fft.rfft(segments * hann, axis=-1)[..., 1:NF + 1]
    real_part = jnp.real(spectrum).astype(jnp.float32)
    imag_part = jnp.imag(spectrum).astype(jnp.float32)
    power = real_part * real_part + imag_part * imag_part
    magnitude = jnp.sqrt(power)
    level = jnp.sqrt(lax.optimization_barrier(jnp.mean(power, axis=-1, keepdims=True)) + 1e-06)
    denom = jnp.maximum(magnitude, 0.3 * level)
    whitened = jnp.concatenate([real_part / denom, imag_part / denom], axis=-1)
    return jnp.transpose(whitened.astype(jnp.bfloat16), (1, 0, 2))

def lag_table():
    freqs = jnp.arange(1, NF + 1).astype(jnp.int32)
    lags = jnp.arange(LAGS).astype(jnp.int32) - LAGS // 2
    phase = freqs[:, None] * lags[None, :] % NW
    theta = 2.0 * math.pi * phase.astype(jnp.float32) / NW
    return (jnp.concatenate([jnp.cos(theta), -jnp.sin(theta)], axis=0) / NF).astype(jnp.bfloat16)

def reference(traces, good_mask):
    whitened = whiten_all(traces, good_mask)
    table_rounded = lax.optimization_barrier(lag_table())
    table = table_rounded.astype(jnp.float32)
    other_real = whitened[..., :NF].astype(jnp.float32)
    other_imag = whitened[..., NF:].astype(jnp.float32)

    def one_block(block):
        own = lax.dynamic_slice_in_dim(whitened, block * CH_DEV, CH_DEV, 1)
        own_real = own[..., :NF].astype(jnp.float32)
        own_imag = own[..., NF:].astype(jnp.float32)
        real_sum = jnp.einsum('wif,wjf->ijf', own_real, other_real) + jnp.einsum('wif,wjf->ijf', own_imag, other_imag)
        imag_sum = jnp.einsum('wif,wjf->ijf', own_imag, other_real) - jnp.einsum('wif,wjf->ijf', own_real, other_imag)
        stack = (jnp.concatenate([real_sum, imag_sum], axis=2) / NWIN).astype(jnp.bfloat16)
        stack = lax.optimization_barrier(stack)
        result = jnp.einsum('ijk,kl->ilj', stack.astype(jnp.float32), table, precision=lax.Precision.HIGHEST)
        return result.astype(jnp.bfloat16)
    blocks = lax.map(one_block, jnp.arange(CHANNELS // CH_DEV).astype(jnp.int32))
    return blocks.reshape(CHANNELS, LAGS, CHANNELS)
```

```python
import math

import jax
import jax.numpy as jnp
from jax import lax
from jax.sharding import PartitionSpec as P

NW = 256
NF = 128
HOP = 128
LAGS = 64
NWIN = 8


def forward_table(width, bins):
    samples = jnp.arange(width)
    freqs = jnp.arange(1, bins + 1)
    phase = samples[:, None] * freqs[None, :] % width
    theta = 2.0 * math.pi * phase.astype(jnp.float32) / width
    hann = 0.5 - 0.5 * jnp.cos(2.0 * math.pi * samples.astype(jnp.float32) / width)
    return jnp.concatenate(
        [hann[:, None] * jnp.cos(theta), -hann[:, None] * jnp.sin(theta)], axis=1
    )


def lag_rotation(width, bins, lag_count):
    freqs = jnp.arange(1, bins + 1)
    lags = jnp.arange(lag_count) - lag_count // 2
    phase = freqs[:, None] * lags[None, :] % width
    theta = 2.0 * math.pi * phase.astype(jnp.float32) / width
    return jnp.cos(theta), jnp.sin(theta)


def whiten(traces, good_mask):
    channels_here = traces.shape[0]
    good = good_mask.astype(jnp.float32)
    total, count = lax.psum((jnp.sum(traces * good[:, None], axis=0), jnp.sum(good)), "chan")
    common = total / jnp.maximum(count, 1.0)
    clean = (traces - common[None, :]) * good[:, None]
    halves = clean.reshape(channels_here, NWIN + 1, HOP)
    segments = jnp.concatenate([halves[:, :-1], halves[:, 1:]], axis=2)
    spectrum = jnp.einsum(
        "cwn,nk->wck", segments, forward_table(NW, NF), precision=lax.Precision.HIGHEST
    )
    real_part = spectrum[..., :NF]
    imag_part = spectrum[..., NF:]
    power = real_part * real_part + imag_part * imag_part
    magnitude = jnp.sqrt(power)
    level = jnp.sqrt(jnp.mean(power, axis=-1, keepdims=True) + 1e-06)
    denom = jnp.maximum(magnitude, 0.3 * level)
    return jnp.concatenate([real_part / denom, imag_part / denom], axis=-1).astype(jnp.bfloat16)


def shards(traces, good_mask):
    whitened = whiten(traces, good_mask)
    others = lax.all_gather(whitened, "chan", axis=1, tiled=True)
    own = whitened.astype(jnp.float32)
    own_real, own_imag = own[..., :NF], own[..., NF:]
    cos, sin = lag_rotation(NW, NF, LAGS)
    scale = 1.0 / (NWIN * NF)
    cos = cos * scale
    sin = sin * scale
    rot_real = own_real[:, :, None, :] * cos.T[None, None] - own_imag[:, :, None, :] * sin.T[None, None]
    rot_imag = own_real[:, :, None, :] * sin.T[None, None] + own_imag[:, :, None, :] * cos.T[None, None]
    rotated = jnp.concatenate([rot_real, rot_imag], axis=-1).astype(jnp.bfloat16)
    result = jnp.einsum(
        "wilk,wjk->ilj", rotated, others, preferred_element_type=jnp.float32
    )
    return result.astype(jnp.bfloat16)


def solution(mesh):
    placed = (P(("groups", "chan"), None), P(("groups", "chan")))
    return jax.shard_map(
        shards,
        mesh=mesh,
        in_specs=placed,
        out_specs=P(("groups", "chan"), None, None),
        check_vma=False,
    )
```

```python
import math

import jax
import jax.numpy as jnp
from jax import lax
from jax.sharding import PartitionSpec as P

NW = 256
NF = 128
HOP = 128
LAGS = 64
NWIN = 8


def butterfly_sum(value, axis, order):
    size = lax.axis_size(axis)
    steps = []
    step = 1
    while step < size:
        steps.append(step)
        step *= 2
    if order == "far":
        steps = steps[::-1]
    for step in steps:
        pairs = [(i, i ^ step) for i in range(size)]
        value = value + lax.ppermute(value, axis, pairs)
    return value


def forward_table(width, bins):
    samples = jnp.arange(width)
    freqs = jnp.arange(1, bins + 1)
    phase = samples[:, None] * freqs[None, :] % width
    theta = 2.0 * math.pi * phase.astype(jnp.float32) / width
    hann = 0.5 - 0.5 * jnp.cos(2.0 * math.pi * samples.astype(jnp.float32) / width)
    return jnp.concatenate(
        [hann[:, None] * jnp.cos(theta), -hann[:, None] * jnp.sin(theta)], axis=1
    )


def lag_rotation(width, bins, lag_count):
    freqs = jnp.arange(1, bins + 1)
    lags = jnp.arange(lag_count) - lag_count // 2
    phase = freqs[:, None] * lags[None, :] % width
    theta = 2.0 * math.pi * phase.astype(jnp.float32) / width
    return jnp.cos(theta), jnp.sin(theta)


def whiten(traces, good_mask):
    channels_here = traces.shape[0]
    good = good_mask.astype(jnp.float32)
    part = jnp.concatenate([jnp.sum(traces * good[:, None], axis=0), jnp.sum(good)[None]])
    summed = butterfly_sum(part, "chan", "far")
    total, count = summed[:-1], summed[-1]
    common = total / jnp.maximum(count, 1.0)
    clean = (traces - common[None, :]) * good[:, None]
    halves = clean.reshape(channels_here, NWIN + 1, HOP)
    segments = jnp.concatenate([halves[:, :-1], halves[:, 1:]], axis=2)
    spectrum = jnp.einsum(
        "cwn,nk->wck", segments, forward_table(NW, NF), precision=lax.Precision.HIGHEST
    )
    real_part = spectrum[..., :NF]
    imag_part = spectrum[..., NF:]
    power = real_part * real_part + imag_part * imag_part
    magnitude = jnp.sqrt(power)
    level = jnp.sqrt(jnp.mean(power, axis=-1, keepdims=True) + 1e-06)
    denom = jnp.maximum(magnitude, 0.3 * level)
    return jnp.concatenate([real_part / denom, imag_part / denom], axis=-1).astype(jnp.bfloat16)


def shards(traces, good_mask):
    whitened = whiten(traces, good_mask)
    others = lax.all_gather(whitened, "chan", axis=1, tiled=True)
    own = whitened.astype(jnp.float32)
    own_real, own_imag = own[..., :NF], own[..., NF:]
    cos, sin = lag_rotation(NW, NF, LAGS)
    scale = 1.0 / (NWIN * NF)
    cos = cos * scale
    sin = sin * scale
    rot_real = own_real[:, :, None, :] * cos.T[None, None] - own_imag[:, :, None, :] * sin.T[None, None]
    rot_imag = own_real[:, :, None, :] * sin.T[None, None] + own_imag[:, :, None, :] * cos.T[None, None]
    rotated = jnp.concatenate([rot_real, rot_imag], axis=-1).astype(jnp.bfloat16)
    result = jnp.einsum(
        "wilk,wjk->ilj", rotated, others, preferred_element_type=jnp.float32
    )
    return result.astype(jnp.bfloat16)


def solution(mesh):
    placed = (P(("groups", "chan"), None), P(("groups", "chan")))
    return jax.shard_map(
        shards,
        mesh=mesh,
        in_specs=placed,
        out_specs=P(("groups", "chan"), None, None),
        check_vma=False,
    )
```

```python
import functools
import math

import jax
import jax.numpy as jnp
from jax import lax
from jax.sharding import PartitionSpec as P

NW = 256
NF = 128
HOP = 128
LAGS = 64
NWIN = 8


def butterfly_sum(value, axis, order):
    size = lax.axis_size(axis)
    steps = []
    step = 1
    while step < size:
        steps.append(step)
        step *= 2
    if order == "far":
        steps = steps[::-1]
    for step in steps:
        pairs = [(i, i ^ step) for i in range(size)]
        value = value + lax.ppermute(value, axis, pairs)
    return value


def forward_table(width, bins):
    samples = jnp.arange(width)
    freqs = jnp.arange(1, bins + 1)
    phase = samples[:, None] * freqs[None, :] % width
    theta = 2.0 * math.pi * phase.astype(jnp.float32) / width
    hann = 0.5 - 0.5 * jnp.cos(2.0 * math.pi * samples.astype(jnp.float32) / width)
    return jnp.concatenate(
        [hann[:, None] * jnp.cos(theta), -hann[:, None] * jnp.sin(theta)], axis=1
    )


def lag_rotation(width, bins, lag_count):
    freqs = jnp.arange(1, bins + 1)
    lags = jnp.arange(lag_count) - lag_count // 2
    phase = freqs[:, None] * lags[None, :] % width
    theta = 2.0 * math.pi * phase.astype(jnp.float32) / width
    return jnp.cos(theta), jnp.sin(theta)


def whiten(traces, good_mask):
    channels_here = traces.shape[0]
    good = good_mask.astype(jnp.float32)
    part = jnp.concatenate([jnp.sum(traces * good[:, None], axis=0), jnp.sum(good)[None]])
    summed = butterfly_sum(part, "chan", "far")
    total, count = summed[:-1], summed[-1]
    common = total / jnp.maximum(count, 1.0)
    clean = (traces - common[None, :]) * good[:, None]
    halves = clean.reshape(channels_here, NWIN + 1, HOP)
    segments = jnp.concatenate([halves[:, :-1], halves[:, 1:]], axis=2)
    spectrum = jnp.einsum(
        "cwn,nk->wck", segments, forward_table(NW, NF), precision=lax.Precision.HIGHEST
    )
    real_part = spectrum[..., :NF]
    imag_part = spectrum[..., NF:]
    power = real_part * real_part + imag_part * imag_part
    magnitude = jnp.sqrt(power)
    level = jnp.sqrt(jnp.mean(power, axis=-1, keepdims=True) + 1e-06)
    denom = jnp.maximum(magnitude, 0.3 * level)
    return jnp.concatenate([real_part / denom, imag_part / denom], axis=-1).astype(jnp.bfloat16)


def ring_plan(mesh):
    row = list(mesh.devices.reshape(-1, mesh.devices.shape[-1])[0])
    size = len(row)
    coords = [tuple(getattr(d, "coords", (0, 0, i // 2))) for i, d in enumerate(row)]
    cores = [getattr(d, "core_on_chip", i % 2) for i, d in enumerate(row)]
    chips = size // 2
    paired = size % 2 == 0 and all(
        coords[2 * k] == coords[2 * k + 1] and cores[2 * k] == 0 and cores[2 * k + 1] == 1
        for k in range(chips)
    )
    if not paired:
        return None
    places = [coords[2 * k] for k in range(chips)]
    ys = sorted({p[1] for p in places})
    if len(ys) == 2:
        lower = sorted((k for k in range(chips) if places[k][1] == ys[0]), key=lambda k: places[k][2])
        upper = sorted((k for k in range(chips) if places[k][1] == ys[1]), key=lambda k: -places[k][2])
        cycle = lower + upper
    else:
        cycle = sorted(range(chips), key=lambda k: (places[k][1], places[k][2], places[k][0]))
    position = {k: p for p, k in enumerate(cycle)}
    return size, chips, cycle, position


def correlate(whitened, rotated, plan):
    size, chips, cycle, position = plan
    here = whitened.shape[1]
    me = lax.axis_index("chan")
    my_chip = me // 2
    is_first_core = (me % 2) == 0

    def shifted(k, s):
        return cycle[(position[k] + s) % chips]

    def pairs(s):
        return [(i, 2 * shifted(i // 2, s) + i % 2) for i in range(size)]

    partner = [(i, i ^ 1) for i in range(size)]
    forward, backward = pairs(1), pairs(-1)
    forward_hops, backward_hops = chips // 2, (chips - 1) // 2
    result = jnp.zeros((rotated.shape[1], rotated.shape[2], size * here), jnp.bfloat16)

    def chip_block(mine, other):
        first = jnp.where(is_first_core, mine, other)
        second = jnp.where(is_first_core, other, mine)
        return jnp.concatenate([first, second], axis=1)

    def emit(result, pieces):
        rhs = jnp.concatenate([block for _, block in pieces], axis=1)
        out = jnp.einsum("wilk,wjk->ilj", rotated, rhs, preferred_element_type=jnp.float32)
        out = out.astype(jnp.bfloat16)
        for t, (table, _) in enumerate(pieces):
            chip = jnp.asarray(table, jnp.int32)[my_chip]
            piece = out[:, :, t * 2 * here:(t + 1) * 2 * here]
            result = lax.dynamic_update_slice(result, piece, (0, 0, chip * 2 * here))
        return result

    own_partner = lax.ppermute(whitened, "chan", partner)
    ahead = lax.ppermute(whitened, "chan", forward)
    behind = lax.ppermute(whitened, "chan", backward) if backward_hops else None
    result = emit(result, [(list(range(chips)), chip_block(whitened, own_partner))])
    for s in range(1, forward_hops + 1):
        ahead_partner = lax.ppermute(ahead, "chan", partner)
        pieces = [([shifted(k, -s) for k in range(chips)], None)]
        behind_partner = None
        if s <= backward_hops:
            behind_partner = lax.ppermute(behind, "chan", partner)
        next_ahead = lax.ppermute(ahead, "chan", forward) if s < forward_hops else None
        next_behind = lax.ppermute(behind, "chan", backward) if s < backward_hops else None
        pieces = [([shifted(k, -s) for k in range(chips)], chip_block(ahead, ahead_partner))]
        if s <= backward_hops:
            pieces.append(([shifted(k, s) for k in range(chips)], chip_block(behind, behind_partner)))
        result = emit(result, pieces)
        ahead, behind = next_ahead, next_behind
    return result


def rotate(whitened):
    own = whitened.astype(jnp.float32)
    own_real, own_imag = own[..., :NF], own[..., NF:]
    cos, sin = lag_rotation(NW, NF, LAGS)
    scale = 1.0 / (NWIN * NF)
    cos = cos * scale
    sin = sin * scale
    rot_real = own_real[:, :, None, :] * cos.T[None, None] - own_imag[:, :, None, :] * sin.T[None, None]
    rot_imag = own_real[:, :, None, :] * sin.T[None, None] + own_imag[:, :, None, :] * cos.T[None, None]
    return jnp.concatenate([rot_real, rot_imag], axis=-1).astype(jnp.bfloat16)


def shards(traces, good_mask, plan=None):
    whitened = whiten(traces, good_mask)
    rotated = rotate(whitened)
    if plan is not None:
        return correlate(whitened, rotated, plan)
    others = lax.all_gather(whitened, "chan", axis=1, tiled=True)
    result = jnp.einsum(
        "wilk,wjk->ilj", rotated, others, preferred_element_type=jnp.float32
    )
    return result.astype(jnp.bfloat16)


def solution(mesh):
    placed = (P(("groups", "chan"), None), P(("groups", "chan")))
    plan = ring_plan(mesh)
    return jax.shard_map(
        functools.partial(shards, plan=plan),
        mesh=mesh,
        in_specs=placed,
        out_specs=P(("groups", "chan"), None, None),
        check_vma=False,
    )
```

```python
import functools
import math

import jax
import jax.numpy as jnp
from jax import lax
from jax.sharding import PartitionSpec as P

NW = 256
NF = 128
HOP = 128
LAGS = 64
NWIN = 8


def butterfly_sum(value, axis, order):
    size = lax.axis_size(axis)
    steps = []
    step = 1
    while step < size:
        steps.append(step)
        step *= 2
    if order == "far":
        steps = steps[::-1]
    for step in steps:
        pairs = [(i, i ^ step) for i in range(size)]
        value = value + lax.ppermute(value, axis, pairs)
    return value


def forward_table(width, bins):
    samples = jnp.arange(width)
    freqs = jnp.arange(1, bins + 1)
    phase = samples[:, None] * freqs[None, :] % width
    theta = 2.0 * math.pi * phase.astype(jnp.float32) / width
    hann = 0.5 - 0.5 * jnp.cos(2.0 * math.pi * samples.astype(jnp.float32) / width)
    return jnp.concatenate(
        [hann[:, None] * jnp.cos(theta), -hann[:, None] * jnp.sin(theta)], axis=1
    )


def lag_rotation(width, bins, lag_count):
    freqs = jnp.arange(1, bins + 1)
    lags = jnp.arange(lag_count) - lag_count // 2
    phase = freqs[:, None] * lags[None, :] % width
    theta = 2.0 * math.pi * phase.astype(jnp.float32) / width
    return jnp.cos(theta), jnp.sin(theta)


def whiten(traces, good_mask):
    channels_here = traces.shape[0]
    good = good_mask.astype(jnp.float32)
    part = jnp.concatenate([jnp.sum(traces * good[:, None], axis=0), jnp.sum(good)[None]])
    summed = butterfly_sum(part, "chan", "far")
    total, count = summed[:-1], summed[-1]
    common = total / jnp.maximum(count, 1.0)
    clean = (traces - common[None, :]) * good[:, None]
    halves = clean.reshape(channels_here, NWIN + 1, HOP)
    segments = jnp.concatenate([halves[:, :-1], halves[:, 1:]], axis=2)
    spectrum = jnp.einsum(
        "cwn,nk->wck", segments, forward_table(NW, NF), precision=lax.Precision.HIGHEST
    )
    real_part = spectrum[..., :NF]
    imag_part = spectrum[..., NF:]
    power = real_part * real_part + imag_part * imag_part
    magnitude = jnp.sqrt(power)
    level = jnp.sqrt(jnp.mean(power, axis=-1, keepdims=True) + 1e-06)
    denom = jnp.maximum(magnitude, 0.3 * level)
    return jnp.concatenate([real_part / denom, imag_part / denom], axis=-1).astype(jnp.bfloat16)


def ring_plan(mesh):
    row = list(mesh.devices.reshape(-1, mesh.devices.shape[-1])[0])
    size = len(row)
    coords = [tuple(getattr(d, "coords", (0, 0, i // 2))) for i, d in enumerate(row)]
    cores = [getattr(d, "core_on_chip", i % 2) for i, d in enumerate(row)]
    chips = size // 2
    paired = size % 2 == 0 and all(
        coords[2 * k] == coords[2 * k + 1] and cores[2 * k] == 0 and cores[2 * k + 1] == 1
        for k in range(chips)
    )
    if not paired:
        return None
    places = [coords[2 * k] for k in range(chips)]
    ys = sorted({p[1] for p in places})
    if len(ys) == 2:
        lower = sorted((k for k in range(chips) if places[k][1] == ys[0]), key=lambda k: places[k][2])
        upper = sorted((k for k in range(chips) if places[k][1] == ys[1]), key=lambda k: -places[k][2])
        cycle = lower + upper
    else:
        cycle = sorted(range(chips), key=lambda k: (places[k][1], places[k][2], places[k][0]))
    position = {k: p for p, k in enumerate(cycle)}
    return size, chips, cycle, position


def correlate(whitened, rotated, plan):
    size, chips, cycle, position = plan
    here = whitened.shape[1]
    me = lax.axis_index("chan")
    my_chip = me // 2
    is_first_core = (me % 2) == 0

    def shifted(k, s):
        return cycle[(position[k] + s) % chips]

    def pairs(s):
        return [(i, 2 * shifted(i // 2, s) + i % 2) for i in range(size)]

    partner = [(i, i ^ 1) for i in range(size)]
    forward, backward = pairs(1), pairs(-1)
    forward_hops, backward_hops = chips // 2, (chips - 1) // 2
    result = jnp.zeros((rotated.shape[1], rotated.shape[2], size * here), jnp.bfloat16)

    def chip_block(mine, other):
        first = jnp.where(is_first_core, mine, other)
        second = jnp.where(is_first_core, other, mine)
        return jnp.concatenate([first, second], axis=1)

    shifts = [0] + [s for h in range(1, forward_hops + 1) for s in ((-h, h) if h <= backward_hops else (-h,))]
    table = jnp.asarray([[shifted(k, s) for s in shifts] for k in range(chips)], jnp.int32)
    placed_chips = table[my_chip]
    slot = {s: n for n, s in enumerate(shifts)}

    def emit(result, pieces):
        rhs = jnp.concatenate([block for _, block in pieces], axis=1)
        out = jnp.einsum("wilk,wjk->ilj", rotated, rhs, preferred_element_type=jnp.float32)
        out = out.astype(jnp.bfloat16)
        for t, (s, _) in enumerate(pieces):
            chip = placed_chips[slot[s]]
            piece = out[:, :, t * 2 * here:(t + 1) * 2 * here]
            result = lax.dynamic_update_slice(result, piece, (0, 0, chip * 2 * here))
        return result

    own_partner = lax.ppermute(whitened, "chan", partner)
    ahead = lax.ppermute(whitened, "chan", forward)
    behind = lax.ppermute(whitened, "chan", backward) if backward_hops else None
    result = emit(result, [(0, chip_block(whitened, own_partner))])
    for s in range(1, forward_hops + 1):
        ahead_partner = lax.ppermute(ahead, "chan", partner)
        behind_partner = None
        if s <= backward_hops:
            behind_partner = lax.ppermute(behind, "chan", partner)
        next_ahead = lax.ppermute(ahead, "chan", forward) if s < forward_hops else None
        next_behind = lax.ppermute(behind, "chan", backward) if s < backward_hops else None
        pieces = [(-s, chip_block(ahead, ahead_partner))]
        if s <= backward_hops:
            pieces.append((s, chip_block(behind, behind_partner)))
        result = emit(result, pieces)
        ahead, behind = next_ahead, next_behind
    return result


def rotate(whitened):
    own = whitened.astype(jnp.float32)
    own_real, own_imag = own[..., :NF], own[..., NF:]
    cos, sin = lag_rotation(NW, NF, LAGS)
    scale = 1.0 / (NWIN * NF)
    cos = cos * scale
    sin = sin * scale
    rot_real = own_real[:, :, None, :] * cos.T[None, None] - own_imag[:, :, None, :] * sin.T[None, None]
    rot_imag = own_real[:, :, None, :] * sin.T[None, None] + own_imag[:, :, None, :] * cos.T[None, None]
    return jnp.concatenate([rot_real, rot_imag], axis=-1).astype(jnp.bfloat16)


def shards(traces, good_mask, plan=None):
    whitened = whiten(traces, good_mask)
    rotated = rotate(whitened)
    if plan is not None:
        return correlate(whitened, rotated, plan)
    others = lax.all_gather(whitened, "chan", axis=1, tiled=True)
    result = jnp.einsum(
        "wilk,wjk->ilj", rotated, others, preferred_element_type=jnp.float32
    )
    return result.astype(jnp.bfloat16)


def solution(mesh):
    placed = (P(("groups", "chan"), None), P(("groups", "chan")))
    plan = ring_plan(mesh)
    return jax.shard_map(
        functools.partial(shards, plan=plan),
        mesh=mesh,
        in_specs=placed,
        out_specs=P(("groups", "chan"), None, None),
        check_vma=False,
    )
```

```python
import functools
import math

import jax
import jax.numpy as jnp
from jax import lax
from jax.sharding import PartitionSpec as P

NW = 256
NF = 128
HOP = 128
LAGS = 64
NWIN = 8


def butterfly_sum(value, axis, order):
    size = lax.axis_size(axis)
    steps = []
    step = 1
    while step < size:
        steps.append(step)
        step *= 2
    if order == "far":
        steps = steps[::-1]
    for step in steps:
        pairs = [(i, i ^ step) for i in range(size)]
        value = value + lax.ppermute(value, axis, pairs)
    return value


def forward_table(width, bins):
    samples = jnp.arange(width)
    freqs = jnp.arange(1, bins + 1)
    phase = samples[:, None] * freqs[None, :] % width
    theta = 2.0 * math.pi * phase.astype(jnp.float32) / width
    hann = 0.5 - 0.5 * jnp.cos(2.0 * math.pi * samples.astype(jnp.float32) / width)
    return jnp.concatenate(
        [hann[:, None] * jnp.cos(theta), -hann[:, None] * jnp.sin(theta)], axis=1
    )


def lag_rotation(width, bins, lag_count):
    freqs = jnp.arange(1, bins + 1)
    lags = jnp.arange(lag_count) - lag_count // 2
    phase = freqs[:, None] * lags[None, :] % width
    theta = 2.0 * math.pi * phase.astype(jnp.float32) / width
    return jnp.cos(theta), jnp.sin(theta)


def whiten(traces, good_mask):
    channels_here = traces.shape[0]
    good = good_mask.astype(jnp.float32)
    part = jnp.concatenate([jnp.sum(traces * good[:, None], axis=0), jnp.sum(good)[None]])
    summed = butterfly_sum(part, "chan", "far")
    total, count = summed[:-1], summed[-1]
    common = total / jnp.maximum(count, 1.0)
    clean = (traces - common[None, :]) * good[:, None]
    halves = clean.reshape(channels_here, NWIN + 1, HOP)
    segments = jnp.concatenate([halves[:, :-1], halves[:, 1:]], axis=2)
    spectrum = jnp.einsum(
        "cwn,nk->wck", segments, forward_table(NW, NF), precision=lax.Precision.HIGHEST
    )
    real_part = spectrum[..., :NF]
    imag_part = spectrum[..., NF:]
    power = real_part * real_part + imag_part * imag_part
    magnitude = jnp.sqrt(power)
    level = jnp.sqrt(jnp.mean(power, axis=-1, keepdims=True) + 1e-06)
    denom = jnp.maximum(magnitude, 0.3 * level)
    return jnp.concatenate([real_part / denom, imag_part / denom], axis=-1).astype(jnp.bfloat16)


def ring_plan(mesh):
    row = list(mesh.devices.reshape(-1, mesh.devices.shape[-1])[0])
    size = len(row)
    coords = [tuple(getattr(d, "coords", (0, 0, i // 2))) for i, d in enumerate(row)]
    cores = [getattr(d, "core_on_chip", i % 2) for i, d in enumerate(row)]
    chips = size // 2
    paired = size % 2 == 0 and all(
        coords[2 * k] == coords[2 * k + 1] and cores[2 * k] == 0 and cores[2 * k + 1] == 1
        for k in range(chips)
    )
    if not paired:
        return None
    places = [coords[2 * k] for k in range(chips)]
    ys = sorted({p[1] for p in places})
    if len(ys) == 2:
        lower = sorted((k for k in range(chips) if places[k][1] == ys[0]), key=lambda k: places[k][2])
        upper = sorted((k for k in range(chips) if places[k][1] == ys[1]), key=lambda k: -places[k][2])
        cycle = lower + upper
    else:
        cycle = sorted(range(chips), key=lambda k: (places[k][1], places[k][2], places[k][0]))
    position = {k: p for p, k in enumerate(cycle)}
    return size, chips, cycle, position


def pick(values, index):
    chosen = jnp.int32(values[0])
    for n in range(1, len(values)):
        chosen = jnp.where(index == n, jnp.int32(values[n]), chosen)
    return chosen


def correlate(whitened, rotated, plan):
    size, chips, cycle, position = plan
    here = whitened.shape[1]
    me = lax.axis_index("chan")
    my_chip = me // 2
    is_first_core = (me % 2) == 0

    def shifted(k, s):
        return cycle[(position[k] + s) % chips]

    def pairs(s):
        return [(i, 2 * shifted(i // 2, s) + i % 2) for i in range(size)]

    partner = [(i, i ^ 1) for i in range(size)]
    forward, backward = pairs(1), pairs(-1)
    forward_hops, backward_hops = chips // 2, (chips - 1) // 2
    result = jnp.zeros((rotated.shape[1], rotated.shape[2], size * here), jnp.bfloat16)

    def chip_block(mine, other):
        first = jnp.where(is_first_core, mine, other)
        second = jnp.where(is_first_core, other, mine)
        return jnp.concatenate([first, second], axis=1)

    shifts = [0] + [s for h in range(1, forward_hops + 1) for s in ((-h, h) if h <= backward_hops else (-h,))]
    my_position = pick([position[k] for k in range(chips)], my_chip)
    placed_chips = [pick([cycle[(p + s) % chips] for p in range(chips)], my_position) for s in shifts]
    slot = {s: n for n, s in enumerate(shifts)}

    def emit(result, pieces):
        rhs = jnp.concatenate([block for _, block in pieces], axis=1)
        out = jnp.einsum("wilk,wjk->ilj", rotated, rhs, preferred_element_type=jnp.float32)
        out = out.astype(jnp.bfloat16)
        for t, (s, _) in enumerate(pieces):
            chip = placed_chips[slot[s]]
            piece = out[:, :, t * 2 * here:(t + 1) * 2 * here]
            result = lax.dynamic_update_slice(result, piece, (0, 0, chip * 2 * here))
        return result

    own_partner = lax.ppermute(whitened, "chan", partner)
    ahead = lax.ppermute(whitened, "chan", forward)
    behind = lax.ppermute(whitened, "chan", backward) if backward_hops else None
    result = emit(result, [(0, chip_block(whitened, own_partner))])
    for s in range(1, forward_hops + 1):
        ahead_partner = lax.ppermute(ahead, "chan", partner)
        behind_partner = None
        if s <= backward_hops:
            behind_partner = lax.ppermute(behind, "chan", partner)
        next_ahead = lax.ppermute(ahead, "chan", forward) if s < forward_hops else None
        next_behind = lax.ppermute(behind, "chan", backward) if s < backward_hops else None
        pieces = [(-s, chip_block(ahead, ahead_partner))]
        if s <= backward_hops:
            pieces.append((s, chip_block(behind, behind_partner)))
        result = emit(result, pieces)
        ahead, behind = next_ahead, next_behind
    return result


def rotate(whitened):
    own = whitened.astype(jnp.float32)
    own_real, own_imag = own[..., :NF], own[..., NF:]
    cos, sin = lag_rotation(NW, NF, LAGS)
    scale = 1.0 / (NWIN * NF)
    cos = cos * scale
    sin = sin * scale
    rot_real = own_real[:, :, None, :] * cos.T[None, None] - own_imag[:, :, None, :] * sin.T[None, None]
    rot_imag = own_real[:, :, None, :] * sin.T[None, None] + own_imag[:, :, None, :] * cos.T[None, None]
    return jnp.concatenate([rot_real, rot_imag], axis=-1).astype(jnp.bfloat16)


def shards(traces, good_mask, plan=None):
    whitened = whiten(traces, good_mask)
    rotated = rotate(whitened)
    if plan is not None:
        return correlate(whitened, rotated, plan)
    others = lax.all_gather(whitened, "chan", axis=1, tiled=True)
    result = jnp.einsum(
        "wilk,wjk->ilj", rotated, others, preferred_element_type=jnp.float32
    )
    return result.astype(jnp.bfloat16)


def solution(mesh):
    placed = (P(("groups", "chan"), None), P(("groups", "chan")))
    plan = ring_plan(mesh)
    return jax.shard_map(
        functools.partial(shards, plan=plan),
        mesh=mesh,
        in_specs=placed,
        out_specs=P(("groups", "chan"), None, None),
        check_vma=False,
    )
```

```python
import functools
import math

import jax
import jax.numpy as jnp
from jax import lax
from jax.sharding import PartitionSpec as P

NW = 256
NF = 128
HOP = 128
LAGS = 64
NWIN = 8


def butterfly_sum(value, axis, order):
    size = lax.axis_size(axis)
    steps = []
    step = 1
    while step < size:
        steps.append(step)
        step *= 2
    if order == "far":
        steps = steps[::-1]
    for step in steps:
        pairs = [(i, i ^ step) for i in range(size)]
        value = value + lax.ppermute(value, axis, pairs)
    return value


def forward_table(width, bins):
    samples = jnp.arange(width)
    freqs = jnp.arange(1, bins + 1)
    phase = samples[:, None] * freqs[None, :] % width
    theta = 2.0 * math.pi * phase.astype(jnp.float32) / width
    hann = 0.5 - 0.5 * jnp.cos(2.0 * math.pi * samples.astype(jnp.float32) / width)
    return jnp.concatenate(
        [hann[:, None] * jnp.cos(theta), -hann[:, None] * jnp.sin(theta)], axis=1
    )


def lag_rotation(width, bins, lag_count):
    freqs = jnp.arange(1, bins + 1)
    lags = jnp.arange(lag_count) - lag_count // 2
    phase = freqs[:, None] * lags[None, :] % width
    theta = 2.0 * math.pi * phase.astype(jnp.float32) / width
    return jnp.cos(theta), jnp.sin(theta)


def whiten(traces, good_mask):
    channels_here = traces.shape[0]
    good = good_mask.astype(jnp.float32)
    widened = jnp.concatenate([traces, jnp.ones((traces.shape[0], 1), traces.dtype)], axis=1)
    part = jnp.sum(widened * good[:, None], axis=0)
    summed = butterfly_sum(part, "chan", "far")
    total, count = summed[:-1], summed[-1]
    common = total / jnp.maximum(count, 1.0)
    clean = (traces - common[None, :]) * good[:, None]
    halves = clean.reshape(channels_here, NWIN + 1, HOP)
    segments = jnp.concatenate([halves[:, :-1], halves[:, 1:]], axis=2)
    spectrum = jnp.einsum(
        "cwn,nk->wck", segments, forward_table(NW, NF), precision=lax.Precision.HIGHEST
    )
    real_part = spectrum[..., :NF]
    imag_part = spectrum[..., NF:]
    power = real_part * real_part + imag_part * imag_part
    magnitude = jnp.sqrt(power)
    level = jnp.sqrt(jnp.mean(power, axis=-1, keepdims=True) + 1e-06)
    denom = jnp.maximum(magnitude, 0.3 * level)
    return jnp.concatenate([real_part / denom, imag_part / denom], axis=-1).astype(jnp.bfloat16)


def ring_plan(mesh):
    row = list(mesh.devices.reshape(-1, mesh.devices.shape[-1])[0])
    size = len(row)
    coords = [tuple(getattr(d, "coords", (0, 0, i // 2))) for i, d in enumerate(row)]
    cores = [getattr(d, "core_on_chip", i % 2) for i, d in enumerate(row)]
    chips = size // 2
    paired = size % 2 == 0 and all(
        coords[2 * k] == coords[2 * k + 1] and cores[2 * k] == 0 and cores[2 * k + 1] == 1
        for k in range(chips)
    )
    if not paired:
        return None
    places = [coords[2 * k] for k in range(chips)]
    ys = sorted({p[1] for p in places})
    if len(ys) == 2:
        lower = sorted((k for k in range(chips) if places[k][1] == ys[0]), key=lambda k: places[k][2])
        upper = sorted((k for k in range(chips) if places[k][1] == ys[1]), key=lambda k: -places[k][2])
        cycle = lower + upper
    else:
        cycle = sorted(range(chips), key=lambda k: (places[k][1], places[k][2], places[k][0]))
    position = {k: p for p, k in enumerate(cycle)}
    return size, chips, cycle, position


def pick(values, index):
    chosen = jnp.int32(values[0])
    for n in range(1, len(values)):
        chosen = jnp.where(index == n, jnp.int32(values[n]), chosen)
    return chosen


def correlate(whitened, rotated, plan):
    size, chips, cycle, position = plan
    here = whitened.shape[1]
    me = lax.axis_index("chan")
    my_chip = me // 2
    is_first_core = (me % 2) == 0

    def shifted(k, s):
        return cycle[(position[k] + s) % chips]

    def pairs(s):
        return [(i, 2 * shifted(i // 2, s) + i % 2) for i in range(size)]

    partner = [(i, i ^ 1) for i in range(size)]
    forward, backward = pairs(1), pairs(-1)
    forward_hops, backward_hops = chips // 2, (chips - 1) // 2
    result = jnp.zeros((rotated.shape[1], rotated.shape[2], size * here), jnp.bfloat16)

    def chip_block(mine, other):
        first = jnp.where(is_first_core, mine, other)
        second = jnp.where(is_first_core, other, mine)
        return jnp.concatenate([first, second], axis=1)

    shifts = [0] + [s for h in range(1, forward_hops + 1) for s in ((-h, h) if h <= backward_hops else (-h,))]
    my_position = pick([position[k] for k in range(chips)], my_chip)
    placed_chips = [pick([cycle[(p + s) % chips] for p in range(chips)], my_position) for s in shifts]
    slot = {s: n for n, s in enumerate(shifts)}

    def emit(result, pieces):
        rhs = jnp.concatenate([block for _, block in pieces], axis=1)
        out = jnp.einsum("wilk,wjk->ilj", rotated, rhs, preferred_element_type=jnp.float32)
        out = out.astype(jnp.bfloat16)
        for t, (s, _) in enumerate(pieces):
            chip = placed_chips[slot[s]]
            piece = out[:, :, t * 2 * here:(t + 1) * 2 * here]
            result = lax.dynamic_update_slice(result, piece, (0, 0, chip * 2 * here))
        return result

    own_partner = lax.ppermute(whitened, "chan", partner)
    ahead = lax.ppermute(whitened, "chan", forward)
    behind = lax.ppermute(whitened, "chan", backward) if backward_hops else None
    result = emit(result, [(0, chip_block(whitened, own_partner))])
    for s in range(1, forward_hops + 1):
        ahead_partner = lax.ppermute(ahead, "chan", partner)
        behind_partner = None
        if s <= backward_hops:
            behind_partner = lax.ppermute(behind, "chan", partner)
        next_ahead = lax.ppermute(ahead, "chan", forward) if s < forward_hops else None
        next_behind = lax.ppermute(behind, "chan", backward) if s < backward_hops else None
        pieces = [(-s, chip_block(ahead, ahead_partner))]
        if s <= backward_hops:
            pieces.append((s, chip_block(behind, behind_partner)))
        result = emit(result, pieces)
        ahead, behind = next_ahead, next_behind
    return result


def rotate(whitened):
    own = whitened.astype(jnp.float32)
    own_real, own_imag = own[..., :NF], own[..., NF:]
    cos, sin = lag_rotation(NW, NF, LAGS)
    scale = 1.0 / (NWIN * NF)
    cos = cos * scale
    sin = sin * scale
    rot_real = own_real[:, :, None, :] * cos.T[None, None] - own_imag[:, :, None, :] * sin.T[None, None]
    rot_imag = own_real[:, :, None, :] * sin.T[None, None] + own_imag[:, :, None, :] * cos.T[None, None]
    return jnp.concatenate([rot_real, rot_imag], axis=-1).astype(jnp.bfloat16)


def shards(traces, good_mask, plan=None):
    whitened = whiten(traces, good_mask)
    rotated = rotate(whitened)
    if plan is not None:
        return correlate(whitened, rotated, plan)
    others = lax.all_gather(whitened, "chan", axis=1, tiled=True)
    result = jnp.einsum(
        "wilk,wjk->ilj", rotated, others, preferred_element_type=jnp.float32
    )
    return result.astype(jnp.bfloat16)


def solution(mesh):
    placed = (P(("groups", "chan"), None), P(("groups", "chan")))
    plan = ring_plan(mesh)
    return jax.shard_map(
        functools.partial(shards, plan=plan),
        mesh=mesh,
        in_specs=placed,
        out_specs=P(("groups", "chan"), None, None),
        check_vma=False,
    )
```

```python
import functools
import math

import jax
import jax.numpy as jnp
from jax import lax
from jax.sharding import PartitionSpec as P

NW = 256
NF = 128
HOP = 128
LAGS = 64
NWIN = 8


def butterfly_sum(value, axis, order):
    size = lax.axis_size(axis)
    steps = []
    step = 1
    while step < size:
        steps.append(step)
        step *= 2
    if order == "far":
        steps = steps[::-1]
    for step in steps:
        pairs = [(i, i ^ step) for i in range(size)]
        value = value + lax.ppermute(value, axis, pairs)
    return value


def forward_table(width, bins):
    samples = jnp.arange(width)
    freqs = jnp.arange(1, bins + 1)
    phase = samples[:, None] * freqs[None, :] % width
    theta = 2.0 * math.pi * phase.astype(jnp.float32) / width
    hann = 0.5 - 0.5 * jnp.cos(2.0 * math.pi * samples.astype(jnp.float32) / width)
    return jnp.concatenate(
        [hann[:, None] * jnp.cos(theta), -hann[:, None] * jnp.sin(theta)], axis=1
    )


def lag_rotation(width, bins, lag_count):
    freqs = jnp.arange(1, bins + 1)
    lags = jnp.arange(lag_count) - lag_count // 2
    phase = freqs[:, None] * lags[None, :] % width
    theta = 2.0 * math.pi * phase.astype(jnp.float32) / width
    return jnp.cos(theta), jnp.sin(theta)


def whiten(traces, good_mask):
    channels_here = traces.shape[0]
    good = good_mask.astype(jnp.float32)
    widened = jnp.concatenate([traces, jnp.ones((traces.shape[0], 1), traces.dtype)], axis=1)
    part = jnp.sum(widened * good[:, None], axis=0)
    summed = butterfly_sum(part, "chan", "far")
    total, count = summed[:-1], summed[-1]
    common = total / jnp.maximum(count, 1.0)
    clean = (traces - common[None, :]) * good[:, None]
    halves = clean.reshape(channels_here, NWIN + 1, HOP)
    segments = jnp.concatenate([halves[:, :-1], halves[:, 1:]], axis=2)
    spectrum = jnp.einsum(
        "cwn,nk->wck", segments, forward_table(NW, NF), precision=lax.Precision.HIGHEST
    )
    real_part = spectrum[..., :NF]
    imag_part = spectrum[..., NF:]
    power = real_part * real_part + imag_part * imag_part
    magnitude = jnp.sqrt(power)
    level = jnp.sqrt(jnp.mean(power, axis=-1, keepdims=True) + 1e-06)
    denom = jnp.maximum(magnitude, 0.3 * level)
    return jnp.concatenate([real_part / denom, imag_part / denom], axis=-1).astype(jnp.bfloat16)


def ring_plan(mesh):
    row = list(mesh.devices.reshape(-1, mesh.devices.shape[-1])[0])
    size = len(row)
    coords = [tuple(getattr(d, "coords", (0, 0, i // 2))) for i, d in enumerate(row)]
    cores = [getattr(d, "core_on_chip", i % 2) for i, d in enumerate(row)]
    chips = size // 2
    paired = size % 2 == 0 and all(
        coords[2 * k] == coords[2 * k + 1] and cores[2 * k] == 0 and cores[2 * k + 1] == 1
        for k in range(chips)
    )
    if not paired:
        return None
    places = [coords[2 * k] for k in range(chips)]
    ys = sorted({p[1] for p in places})
    if len(ys) == 2:
        lower = sorted((k for k in range(chips) if places[k][1] == ys[0]), key=lambda k: places[k][2])
        upper = sorted((k for k in range(chips) if places[k][1] == ys[1]), key=lambda k: -places[k][2])
        cycle = lower + upper
    else:
        cycle = sorted(range(chips), key=lambda k: (places[k][1], places[k][2], places[k][0]))
    position = {k: p for p, k in enumerate(cycle)}
    return size, chips, cycle, position


def pick(values, index):
    chosen = jnp.int32(values[0])
    for n in range(1, len(values)):
        chosen = jnp.where(index == n, jnp.int32(values[n]), chosen)
    return chosen


def correlate(whitened, rotated, plan):
    size, chips, cycle, position = plan
    here = whitened.shape[1]
    me = lax.axis_index("chan")
    my_chip = me // 2
    is_first_core = (me % 2) == 0

    def shifted(k, s):
        return cycle[(position[k] + s) % chips]

    def pairs(s):
        return [(i, 2 * shifted(i // 2, s) + i % 2) for i in range(size)]

    partner = [(i, i ^ 1) for i in range(size)]
    forward, backward = pairs(1), pairs(-1)
    forward_hops, backward_hops = chips // 2, (chips - 1) // 2
    result = jnp.zeros((rotated.shape[1], rotated.shape[2], size * here), jnp.bfloat16)

    def chip_block(mine, other):
        first = jnp.where(is_first_core, mine, other)
        second = jnp.where(is_first_core, other, mine)
        return jnp.concatenate([first, second], axis=1)

    shifts = [0] + [s for h in range(1, forward_hops + 1) for s in ((-h, h) if h <= backward_hops else (-h,))]
    my_position = pick([position[k] for k in range(chips)], my_chip)
    placed_chips = [pick([cycle[(p + s) % chips] for p in range(chips)], my_position) for s in shifts]
    slot = {s: n for n, s in enumerate(shifts)}

    def emit(result, pieces):
        rhs = jnp.concatenate([block for _, block in pieces], axis=1)
        out = jnp.einsum("wilk,wjk->ilj", rotated, rhs, preferred_element_type=jnp.float32)
        out = out.astype(jnp.bfloat16)
        for t, (s, _) in enumerate(pieces):
            chip = placed_chips[slot[s]]
            piece = out[:, :, t * 2 * here:(t + 1) * 2 * here]
            result = lax.dynamic_update_slice(result, piece, (0, 0, chip * 2 * here))
        return result

    own_partner = lax.ppermute(whitened, "chan", partner)
    unit = chip_block(whitened, own_partner)
    result = emit(result, [(0, unit)])
    first_core = me % 2 == 0
    for s in range(1, forward_hops + 1):
        both = s <= backward_hops
        ring = [(2 * k, 2 * shifted(k, 1)) for k in range(chips)]
        swap = [(2 * k, 2 * k + 1) for k in range(chips)]
        if both:
            ring += [(2 * k + 1, 2 * shifted(k, -1) + 1) for k in range(chips)]
            swap += [(2 * k + 1, 2 * k) for k in range(chips)]
        unit = lax.ppermute(unit, "chan", ring)
        other = lax.ppermute(unit, "chan", swap)
        if both:
            rhs = jnp.concatenate([unit, other], axis=1)
            out = jnp.einsum("wilk,wjk->ilj", rotated, rhs, preferred_element_type=jnp.float32)
            out = out.astype(jnp.bfloat16)
            mine = jnp.where(first_core, placed_chips[slot[-s]], placed_chips[slot[s]])
            theirs = jnp.where(first_core, placed_chips[slot[s]], placed_chips[slot[-s]])
            for t, chip in enumerate((mine, theirs)):
                piece = out[:, :, t * 2 * here:(t + 1) * 2 * here]
                result = lax.dynamic_update_slice(result, piece, (0, 0, chip * 2 * here))
        else:
            rhs = jnp.where(first_core, unit, other)
            result = emit(result, [(-s, rhs)])
    return result


def rotate(whitened):
    own = whitened.astype(jnp.float32)
    own_real, own_imag = own[..., :NF], own[..., NF:]
    cos, sin = lag_rotation(NW, NF, LAGS)
    scale = 1.0 / (NWIN * NF)
    cos = cos * scale
    sin = sin * scale
    rot_real = own_real[:, :, None, :] * cos.T[None, None] - own_imag[:, :, None, :] * sin.T[None, None]
    rot_imag = own_real[:, :, None, :] * sin.T[None, None] + own_imag[:, :, None, :] * cos.T[None, None]
    return jnp.concatenate([rot_real, rot_imag], axis=-1).astype(jnp.bfloat16)


def shards(traces, good_mask, plan=None):
    whitened = whiten(traces, good_mask)
    rotated = rotate(whitened)
    if plan is not None:
        return correlate(whitened, rotated, plan)
    others = lax.all_gather(whitened, "chan", axis=1, tiled=True)
    result = jnp.einsum(
        "wilk,wjk->ilj", rotated, others, preferred_element_type=jnp.float32
    )
    return result.astype(jnp.bfloat16)


def solution(mesh):
    placed = (P(("groups", "chan"), None), P(("groups", "chan")))
    plan = ring_plan(mesh)
    return jax.shard_map(
        functools.partial(shards, plan=plan),
        mesh=mesh,
        in_specs=placed,
        out_specs=P(("groups", "chan"), None, None),
        check_vma=False,
    )
```

```python
import functools
import math

import jax
import jax.numpy as jnp
from jax import lax
from jax.sharding import PartitionSpec as P

NW = 256
NF = 128
HOP = 128
LAGS = 64
NWIN = 8


def butterfly_sum(value, axis, order):
    size = lax.axis_size(axis)
    steps = []
    step = 1
    while step < size:
        steps.append(step)
        step *= 2
    if order == "far":
        steps = steps[::-1]
    for step in steps:
        pairs = [(i, i ^ step) for i in range(size)]
        value = value + lax.ppermute(value, axis, pairs)
    return value


def forward_table(width, bins):
    samples = jnp.arange(width)
    freqs = jnp.arange(1, bins + 1)
    phase = samples[:, None] * freqs[None, :] % width
    theta = 2.0 * math.pi * phase.astype(jnp.float32) / width
    hann = 0.5 - 0.5 * jnp.cos(2.0 * math.pi * samples.astype(jnp.float32) / width)
    return jnp.concatenate(
        [hann[:, None] * jnp.cos(theta), -hann[:, None] * jnp.sin(theta)], axis=1
    )


def lag_rotation(width, bins, lag_count):
    freqs = jnp.arange(1, bins + 1)
    lags = jnp.arange(lag_count) - lag_count // 2
    phase = freqs[:, None] * lags[None, :] % width
    theta = 2.0 * math.pi * phase.astype(jnp.float32) / width
    return jnp.cos(theta), jnp.sin(theta)


def whiten(traces, good_mask):
    channels_here = traces.shape[0]
    good = good_mask.astype(jnp.float32)
    widened = jnp.concatenate([traces, jnp.ones((traces.shape[0], 1), traces.dtype)], axis=1)
    part = jnp.sum(widened * good[:, None], axis=0)
    summed = butterfly_sum(part, "chan", "far")
    total, count = summed[:-1], summed[-1]
    common = total / jnp.maximum(count, 1.0)
    clean = (traces - common[None, :]) * good[:, None]
    halves = clean.reshape(channels_here, NWIN + 1, HOP)
    segments = jnp.concatenate([halves[:, :-1], halves[:, 1:]], axis=2)
    spectrum = jnp.einsum(
        "cwn,nk->wck", segments, forward_table(NW, NF), precision=lax.Precision.HIGHEST
    )
    real_part = spectrum[..., :NF]
    imag_part = spectrum[..., NF:]
    power = real_part * real_part + imag_part * imag_part
    magnitude = jnp.sqrt(power)
    level = jnp.sqrt(jnp.mean(power, axis=-1, keepdims=True) + 1e-06)
    denom = jnp.maximum(magnitude, 0.3 * level)
    return jnp.concatenate([real_part / denom, imag_part / denom], axis=-1).astype(jnp.bfloat16)


def ring_plan(mesh):
    row = list(mesh.devices.reshape(-1, mesh.devices.shape[-1])[0])
    size = len(row)
    coords = [tuple(getattr(d, "coords", (0, 0, i // 2))) for i, d in enumerate(row)]
    cores = [getattr(d, "core_on_chip", i % 2) for i, d in enumerate(row)]
    chips = size // 2
    paired = size % 2 == 0 and all(
        coords[2 * k] == coords[2 * k + 1] and cores[2 * k] == 0 and cores[2 * k + 1] == 1
        for k in range(chips)
    )
    if not paired:
        return None
    places = [coords[2 * k] for k in range(chips)]
    ys = sorted({p[1] for p in places})
    if len(ys) == 2:
        lower = sorted((k for k in range(chips) if places[k][1] == ys[0]), key=lambda k: places[k][2])
        upper = sorted((k for k in range(chips) if places[k][1] == ys[1]), key=lambda k: -places[k][2])
        cycle = lower + upper
    else:
        cycle = sorted(range(chips), key=lambda k: (places[k][1], places[k][2], places[k][0]))
    position = {k: p for p, k in enumerate(cycle)}
    return size, chips, cycle, position


def pick(values, index):
    chosen = jnp.int32(values[0])
    for n in range(1, len(values)):
        chosen = jnp.where(index == n, jnp.int32(values[n]), chosen)
    return chosen


def correlate(whitened, rotated, plan):
    size, chips, cycle, position = plan
    here = whitened.shape[1]
    me = lax.axis_index("chan")
    my_chip = me // 2
    is_first_core = (me % 2) == 0

    def shifted(k, s):
        return cycle[(position[k] + s) % chips]

    def pairs(s):
        return [(i, 2 * shifted(i // 2, s) + i % 2) for i in range(size)]

    partner = [(i, i ^ 1) for i in range(size)]
    forward, backward = pairs(1), pairs(-1)
    forward_hops, backward_hops = chips // 2, (chips - 1) // 2
    result = jnp.zeros((rotated.shape[1], rotated.shape[2], size * here), jnp.bfloat16)

    def chip_block(mine, other):
        first = jnp.where(is_first_core, mine, other)
        second = jnp.where(is_first_core, other, mine)
        return jnp.concatenate([first, second], axis=1)

    shifts = [0] + [s for h in range(1, forward_hops + 1) for s in ((-h, h) if h <= backward_hops else (-h,))]
    my_position = pick([position[k] for k in range(chips)], my_chip)
    placed_chips = [pick([cycle[(p + s) % chips] for p in range(chips)], my_position) for s in shifts]
    slot = {s: n for n, s in enumerate(shifts)}

    def emit(result, pieces):
        rhs = jnp.concatenate([block for _, block in pieces], axis=1)
        out = jnp.einsum("wilk,wjk->ilj", rotated, rhs, preferred_element_type=jnp.float32)
        out = out.astype(jnp.bfloat16)
        for t, (s, _) in enumerate(pieces):
            chip = placed_chips[slot[s]]
            piece = out[:, :, t * 2 * here:(t + 1) * 2 * here]
            result = lax.dynamic_update_slice(result, piece, (0, 0, chip * 2 * here))
        return result

    own_partner = lax.ppermute(whitened, "chan", partner)
    unit = chip_block(whitened, own_partner)
    result = emit(result, [(0, unit)])
    first_core = me % 2 == 0
    for s in range(1, forward_hops + 1):
        both = s <= backward_hops
        opposite = not both and chips % 2 == 0
        ring = [(2 * k, 2 * shifted(k, 1)) for k in range(chips)]
        swap = [(2 * k, 2 * k + 1) for k in range(chips)]
        if both or opposite:
            ring += [(2 * k + 1, 2 * shifted(k, -1) + 1) for k in range(chips)]
            swap += [(2 * k + 1, 2 * k) for k in range(chips)]
        unit = lax.ppermute(unit, "chan", ring)
        if opposite:
            result = emit(result, [(-s, unit)])
            continue
        other = lax.ppermute(unit, "chan", swap)
        if both:
            rhs = jnp.concatenate([unit, other], axis=1)
            out = jnp.einsum("wilk,wjk->ilj", rotated, rhs, preferred_element_type=jnp.float32)
            out = out.astype(jnp.bfloat16)
            mine = jnp.where(first_core, placed_chips[slot[-s]], placed_chips[slot[s]])
            theirs = jnp.where(first_core, placed_chips[slot[s]], placed_chips[slot[-s]])
            for t, chip in enumerate((mine, theirs)):
                piece = out[:, :, t * 2 * here:(t + 1) * 2 * here]
                result = lax.dynamic_update_slice(result, piece, (0, 0, chip * 2 * here))
        else:
            rhs = jnp.where(first_core, unit, other)
            result = emit(result, [(-s, rhs)])
    return result


def rotate(whitened):
    own = whitened.astype(jnp.float32)
    own_real, own_imag = own[..., :NF], own[..., NF:]
    cos, sin = lag_rotation(NW, NF, LAGS)
    scale = 1.0 / (NWIN * NF)
    cos = cos * scale
    sin = sin * scale
    rot_real = own_real[:, :, None, :] * cos.T[None, None] - own_imag[:, :, None, :] * sin.T[None, None]
    rot_imag = own_real[:, :, None, :] * sin.T[None, None] + own_imag[:, :, None, :] * cos.T[None, None]
    return jnp.concatenate([rot_real, rot_imag], axis=-1).astype(jnp.bfloat16)


def shards(traces, good_mask, plan=None):
    whitened = whiten(traces, good_mask)
    rotated = rotate(whitened)
    if plan is not None:
        return correlate(whitened, rotated, plan)
    others = lax.all_gather(whitened, "chan", axis=1, tiled=True)
    result = jnp.einsum(
        "wilk,wjk->ilj", rotated, others, preferred_element_type=jnp.float32
    )
    return result.astype(jnp.bfloat16)


def solution(mesh):
    placed = (P(("groups", "chan"), None), P(("groups", "chan")))
    plan = ring_plan(mesh)
    return jax.shard_map(
        functools.partial(shards, plan=plan),
        mesh=mesh,
        in_specs=placed,
        out_specs=P(("groups", "chan"), None, None),
        check_vma=False,
    )
```
